512 devices in a mesh: gx: 64 (over z, y), gy: 8 (over x, core).
Axes of the slice: x: 4, y: 4, z: 16, core: 2. Of those that a mesh axis runs over, the one named last changes fastest.
Arguments:
- charges: float32 [1024, 128, 128], P('gx', 'gy'), may hold values from -6 to 6
- kernels: float32 [4, 11, 11, 11], replicated, may hold values from 0 to 0.3, as said below
- top_kernel: float32 [127, 15, 15], replicated, may hold values from 0 to 0.012, as said below
Outputs:
- potential: float32 [1024, 128, 128], P('gx', 'gy')
The draws below stay inside these ranges and needn't reach their ends.
Inputs may be any that keep to these rules, and one draw needn't show every extreme that they name: Positive level kernels; each entry is at most 0.29 / (1 + its offset's distance from the centre), with an independent factor at each offset. `top_kernel`: positive top kernel; each entry is at most 0.0114 / (1 + its offset's distance from the centre), with an independent factor at each offset.
All inputs are finite; a program needn't handle non-finite values.
Results may differ from the reference program's by a relative error of at most 0.0001.
Values sent between devices are 32-bit elements; how exact they have to be, the bound alone decides.
No kernel may reach another device: no remote copies, remote signals or barrier semaphores. Data moves between devices by JAX's collectives and lax.ppermute only.
A program may use at most 64 MiB of HBM per device.

```python
import jax
import jax.numpy as jnp
from jax import lax

NZ = 128
LEVELS = 4
RADIUS = 5
NX = 1024
NY = 128
TOPX = 64
TOPY = 8
TOPZ = 8


def draw_kernels(key, part):
    kernel_span = 2 * RADIUS + 1
    offsets = jnp.arange(kernel_span, dtype=jnp.float32) - RADIUS
    distance = jnp.sqrt(offsets[:, None, None] * offsets[:, None, None] + offsets[None, :, None] * offsets[None, :, None] + offsets[None, None, :] * offsets[None, None, :])
    factor = jax.random.uniform(key, (LEVELS, kernel_span, kernel_span, kernel_span), jnp.float32, 0.5, 1.5)
    scales = 0.15 * jnp.power(0.45, jnp.arange(LEVELS, dtype=jnp.float32))
    return scales[:, None, None, None] * factor / (1.0 + distance[None])


def draw_top_kernel(key, part):
    first_offsets = jnp.arange(2 * TOPX - 1, dtype=jnp.float32) - (TOPX - 1)
    second_offsets = jnp.arange(2 * TOPY - 1, dtype=jnp.float32) - (TOPY - 1)
    third_offsets = jnp.arange(2 * TOPZ - 1, dtype=jnp.float32) - (TOPZ - 1)
    distance = jnp.sqrt(first_offsets[:, None, None] * first_offsets[:, None, None] + second_offsets[None, :, None] * second_offsets[None, :, None] + third_offsets[None, None, :] * third_offsets[None, None, :])
    shape_all = (2 * TOPX - 1, 2 * TOPY - 1, 2 * TOPZ - 1)
    factor = jax.random.uniform(key, shape_all, jnp.float32, 0.5, 1.5)
    return 0.006 * factor / (1.0 + distance)


def level_of(own_key, extent, cuts, low, largest):
    def one(dim, blocks):
        heights = jax.random.uniform(jax.random.fold_in(jax.random.fold_in(own_key, 6), dim), (blocks,), jnp.float32, low / len(cuts), largest / len(cuts))
        return jnp.repeat(jnp.exp(heights), extent[dim] // blocks).reshape((-1,) + (1,) * (len(extent) - dim - 1))

    level = one(*cuts[0])
    for cut in cuts[1:]:
        level = level * one(*cut)
    return level


def normal_values(rng, dims, scale, bound, split=(), held_as=jnp.bfloat16):
    entries = scale * jax.random.normal(rng, dims, jnp.float32)
    if split:
        entries = entries * level_of(rng, dims, split, -0.22, 0.18)
    return jnp.clip(entries, -bound, bound).astype(held_as)


def setup_inputs(seed: int = 0) -> dict:
    key_of = jax.random.split(jax.random.key(seed), 4)
    charges = normal_values(key_of[0], (NX, NY, NZ), 1.0, 6.0, ((0, 64), (1, 8)), jnp.float32)
    kernels = draw_kernels(jax.random.fold_in(key_of[3], 71), 0)
    top_kernel = draw_top_kernel(jax.random.fold_in(key_of[3], 71), 0)
    return dict(charges=charges, kernels=kernels, top_kernel=top_kernel)


def correlate(values_grid, kernel):
    flipped = kernel[::-1, ::-1, ::-1]
    full_shape = tuple(sizes_a + sizes_b - 1 for sizes_a, sizes_b in zip(values_grid.shape, kernel.shape))
    spectrum = jnp.fft.rfftn(values_grid, full_shape) * jnp.fft.rfftn(flipped, full_shape)
    full_result = jnp.fft.irfftn(spectrum, full_shape)
    offsets = [(kernel.shape[index_dim] - 1) // 2 for index_dim in range(3)]
    return full_result[offsets[0]:offsets[0] + values_grid.shape[0], offsets[1]:offsets[1] + values_grid.shape[1], offsets[2]:offsets[2] + values_grid.shape[2]].astype(values_grid.dtype)


def restrict_axis(values_grid, along_axis):
    cell_count = values_grid.shape[along_axis]
    zero_layer = jnp.zeros_like(lax.slice_in_dim(values_grid, 0, 1, axis=along_axis))
    padded = jnp.concatenate([zero_layer, values_grid], axis=along_axis)
    left_cells = lax.slice_in_dim(padded, 0, cell_count, 2, along_axis)
    centre = lax.slice_in_dim(padded, 1, cell_count + 1, 2, along_axis)
    right_cells = lax.slice_in_dim(padded, 2, cell_count + 1, 2, along_axis)
    return 0.5 * left_cells + centre + 0.5 * right_cells


def prolong_axis(coarse, along_axis):
    zero_layer = jnp.zeros_like(lax.slice_in_dim(coarse, 0, 1, axis=along_axis))
    following = jnp.concatenate([lax.slice_in_dim(coarse, 1, coarse.shape[along_axis], axis=along_axis), zero_layer], axis=along_axis)
    middle = 0.5 * (coarse + following)
    paired = jnp.stack([coarse, middle], axis=along_axis + 1)
    new_shape = list(coarse.shape)
    new_shape[along_axis] = 2 * new_shape[along_axis]
    return paired.reshape(new_shape)


def reference(charges, kernels, top_kernel):
    local_terms = []
    current = charges
    for level_index in range(kernels.shape[0]):
        local_terms.append(correlate(current, kernels[level_index]))
        current = restrict_axis(restrict_axis(restrict_axis(current, 0), 1), 2)
    potential = correlate(current, top_kernel)
    for level_index in reversed(range(kernels.shape[0])):
        expanded = prolong_axis(prolong_axis(prolong_axis(potential, 0), 1), 2)
        potential = local_terms[level_index] + expanded
    return potential
```

```python
import jax
import jax.numpy as jnp
from jax import lax
from jax.sharding import PartitionSpec as P

HIGHEST = lax.Precision.HIGHEST


def from_behind(value, axis, steps):
    count = lax.axis_size(axis)
    leading, last = (max(0, -steps), min(count, count - steps))
    pairs = [(source, source + steps) for source in range(leading, last)]
    if not pairs:
        return jnp.zeros_like(value)
    return lax.ppermute(value, axis, pairs)


def take(values, along_axis, start, stop, stride=1):
    return lax.slice_in_dim(values, start, stop, stride, along_axis)


def restrict(values, along_axis, low, out_low, out_high):
    count = out_high - out_low
    first = 2 * out_low - 1 - low
    left = take(values, along_axis, first, first + 2 * count - 1, 2)
    centre = take(values, along_axis, first + 1, first + 2 * count, 2)
    right = take(values, along_axis, first + 2, first + 2 * count + 1, 2)
    return 0.5 * left + centre + 0.5 * right


def restrict_whole(values, along_axis):
    cell_count = values.shape[along_axis]
    zero_layer = jnp.zeros_like(take(values, along_axis, 0, 1))
    padded = jnp.concatenate([zero_layer, values], axis=along_axis)
    left = take(padded, along_axis, 0, cell_count, 2)
    centre = take(padded, along_axis, 1, cell_count + 1, 2)
    right = take(padded, along_axis, 2, cell_count + 1, 2)
    return 0.5 * left + centre + 0.5 * right


def inside_mask(values, along_axis, axis_name, tile, low):
    count = lax.axis_size(axis_name)
    shape = [1] * values.ndim
    shape[along_axis] = values.shape[along_axis]
    local = lax.broadcasted_iota(jnp.int32, tuple(shape), along_axis) + low
    global_index = lax.axis_index(axis_name) * tile + local
    return jnp.where(global_index < count * tile, values, jnp.zeros_like(values))


def prolong(coarse, along_axis, fine_count):
    m = fine_count // 2
    have = coarse.shape[along_axis]
    if have < m + 1:
        coarse = jnp.concatenate(
            [coarse, jnp.zeros_like(take(coarse, along_axis, 0, m + 1 - have))], axis=along_axis
        )
    base = take(coarse, along_axis, 0, m)
    following = take(coarse, along_axis, 1, m + 1)
    middle = 0.5 * (base + following)
    paired = jnp.stack([base, middle], axis=along_axis + 1)
    shape = list(base.shape)
    shape[along_axis] = 2 * m
    fine = paired.reshape(shape)
    if fine_count > 2 * m:
        fine = jnp.concatenate([fine, take(coarse, along_axis, m, m + 1)], axis=along_axis)
    return fine


def banded_weights(kernel, depth):
    span = kernel.shape[2]
    radius = span // 2
    offset = (
        lax.broadcasted_iota(jnp.int32, (depth, depth), 0)
        - lax.broadcasted_iota(jnp.int32, (depth, depth), 1)
        + radius
    )
    weights = jnp.zeros(kernel.shape[:2] + (depth, depth), jnp.float32)
    for c in range(span):
        weights = jnp.where(offset[None, None] == c, kernel[:, :, c][:, :, None, None], weights)
    return weights


def cutoff_sum(window, kernel):
    span = kernel.shape[0]
    rows_first = window.shape[0] - span + 1
    rows_second = window.shape[1] - span + 1
    weights = banded_weights(kernel, window.shape[2])
    stacked = jnp.stack([take(window, 1, b, b + rows_second) for b in range(span)], axis=2)
    accumulated = None
    for a in range(span):
        term = jnp.einsum(
            "xybz,bzw->xyw", take(stacked, 0, a, a + rows_first), weights[a], precision=HIGHEST
        )
        accumulated = term if accumulated is None else accumulated + term
    return accumulated


def widen_many(arrays, along_axis, axis_name, needs):
    tiles = [a.shape[along_axis] for a in arrays]
    reach = 0
    for tile, (low, high) in zip(tiles, needs):
        reach = max(reach, -(-low // tile), -(-high // tile))
    lower = [[] for _ in arrays]
    upper = [[] for _ in arrays]
    for distance in range(1, reach + 1):
        for direction in (1, -1):
            pieces = []
            for index, (a, tile, (low, high)) in enumerate(zip(arrays, tiles, needs)):
                if direction == 1:
                    start = max(0, distance * tile - low)
                    stop = tile if (distance - 1) * tile < low else start
                else:
                    start = 0
                    stop = min(tile, tile + high - distance * tile) if (distance - 1) * tile < high else 0
                if stop > start:
                    pieces.append((index, take(a, along_axis, start, stop)))
            if not pieces:
                continue
            flat = jnp.concatenate([p.reshape(-1) for _, p in pieces])
            moved = from_behind(flat, axis_name, direction * distance)
            offset = 0
            for index, p in pieces:
                size = p.size
                part = moved[offset : offset + size].reshape(p.shape)
                offset += size
                if direction == 1:
                    lower[index].insert(0, part)
                else:
                    upper[index].append(part)
    return [
        jnp.concatenate(lower[i] + [a] + upper[i], axis=along_axis) for i, a in enumerate(arrays)
    ]


def gather_all(value, along_axis, axis_name):
    count = lax.axis_size(axis_name)
    if count & (count - 1):
        return lax.all_gather(value, axis_name, axis=along_axis, tiled=True)
    position = lax.axis_index(axis_name)
    step = 1
    while step < count:
        other = lax.ppermute(value, axis_name, [(i, i ^ step) for i in range(count)])
        low_half = (position // step) % 2 == 0
        value = jnp.where(
            low_half,
            jnp.concatenate([value, other], axis=along_axis),
            jnp.concatenate([other, value], axis=along_axis),
        )
        step *= 2
    return value


def top_cells(whole_top, top_kernel, tile_first, tile_second):
    n_first, n_second, depth = whole_top.shape
    padded = jnp.pad(top_kernel, ((tile_first, 0), (tile_second, 0), (0, 0)))
    start_first = n_first - 1 - lax.axis_index("gx") * tile_first
    start_second = n_second - 1 - lax.axis_index("gy") * tile_second
    window = lax.dynamic_slice(
        padded,
        (start_first, start_second, jnp.int32(0)),
        (n_first + tile_first, n_second + tile_second, 2 * depth - 1),
    )
    rows = []
    for j in range(tile_first + 1):
        cols = []
        for i in range(tile_second + 1):
            deep = []
            for z in range(depth):
                deep.append(
                    window[
                        tile_first - j : tile_first - j + n_first,
                        tile_second - i : tile_second - i + n_second,
                        depth - 1 - z : 2 * depth - 1 - z,
                    ]
                )
            cols.append(jnp.stack(deep))
        rows.append(jnp.stack(cols))
    weights = jnp.stack(rows)
    return jnp.einsum("jizabc,abc->jiz", weights, whole_top, precision=HIGHEST)


def body(charges, kernels, top_kernel):
    levels = kernels.shape[0]
    radius = kernels.shape[1] // 2
    tile0_first, tile0_second, depth0 = charges.shape
    tiles_first = [tile0_first >> l for l in range(levels + 1)]
    tiles_second = [tile0_second >> l for l in range(levels + 1)]

    low1 = min(-radius, -(2 ** (levels - 1) - 1))
    high1 = tiles_first[1] + radius + 1
    high1_second = tiles_second[1] + radius + 1
    low0 = 2 * low1 - 1
    high0 = 2 * (high1 - 1) + 2
    high0_second = 2 * (high1_second - 1) + 2
    assert -low0 <= tile0_first and high0 - tile0_first <= tile0_first
    assert -low0 <= tile0_second and high0_second - tile0_second <= tile0_second

    below = from_behind(take(charges, 0, tile0_first + low0, tile0_first), "gx", 1)
    above = from_behind(take(charges, 0, 0, high0 - tile0_first), "gx", -1)
    wide = jnp.concatenate([below, charges, above], axis=0)
    below = from_behind(take(wide, 1, tile0_second + low0, tile0_second), "gy", 1)
    above = from_behind(take(wide, 1, 0, high0_second - tile0_second), "gy", -1)
    wide = jnp.concatenate([below, wide, above], axis=1)

    q1 = restrict(wide, 0, low0, low1, high1)
    q1 = restrict(q1, 1, low0, low1, high1_second)
    q1 = restrict_whole(q1, 2)
    q1 = inside_mask(q1, 0, "gx", tiles_first[1], low1)
    q1 = inside_mask(q1, 1, "gy", tiles_second[1], low1)

    coarse = [None, q1]
    low = low1
    current = q1
    for l in range(2, levels + 1):
        new_low = -(2 ** (levels - l) - 1)
        current = restrict(current, 0, low, new_low, tiles_first[l])
        current = restrict(current, 1, low, new_low, tiles_second[l])
        current = restrict_whole(current, 2)
        coarse.append(current)
        low = new_low
    q_top = coarse[levels]

    whole_top = gather_all(gather_all(q_top, 1, "gy"), 0, "gx")

    own = [take(take(coarse[l], 0, 2 ** (levels - l) - 1, 2 ** (levels - l) - 1 + tiles_first[l]), 1,
                2 ** (levels - l) - 1, 2 ** (levels - l) - 1 + tiles_second[l]) for l in range(2, levels)]
    widened = widen_many(own, 0, "gx", [(radius, radius + 1)] * len(own))
    widened = widen_many(widened, 1, "gy", [(radius, radius + 1)] * len(own))

    window0 = take(take(wide, 0, -radius - low0, tile0_first + radius - low0), 1, -radius - low0,
                   tile0_second + radius - low0)
    terms = [cutoff_sum(window0, kernels[0])]
    window1 = take(take(q1, 0, -radius - low1, tiles_first[1] + radius + 1 - low1), 1,
                   -radius - low1, tiles_second[1] + radius + 1 - low1)
    terms.append(cutoff_sum(window1, kernels[1]))
    for l in range(2, levels):
        terms.append(cutoff_sum(widened[l - 2], kernels[l]))

    potential = top_cells(whole_top, top_kernel, tiles_first[levels], tiles_second[levels])
    potential = inside_mask(potential, 0, "gx", tiles_first[levels], 0)
    potential = inside_mask(potential, 1, "gy", tiles_second[levels], 0)
    for l in reversed(range(levels)):
        rim = 1 if l > 0 else 0
        expanded = prolong(potential, 0, tiles_first[l] + rim)
        expanded = prolong(expanded, 1, tiles_second[l] + rim)
        expanded = prolong(expanded, 2, depth0 >> l)
        potential = terms[l] + expanded
        if rim:
            potential = inside_mask(potential, 0, "gx", tiles_first[l], 0)
            potential = inside_mask(potential, 1, "gy", tiles_second[l], 0)
    return potential


def solution(mesh):
    in_specs = (P("gx", "gy", None), P(), P())
    out_specs = P("gx", "gy", None)
    return jax.shard_map(body, mesh=mesh, in_specs=in_specs, out_specs=out_specs, check_vma=False)
```

```python
import jax
import jax.numpy as jnp
from jax import lax
from jax.sharding import PartitionSpec as P

HIGHEST = lax.Precision.HIGHEST


def from_behind(value, axis, steps):
    count = lax.axis_size(axis)
    leading, last = (max(0, -steps), min(count, count - steps))
    pairs = [(source, source + steps) for source in range(leading, last)]
    if not pairs:
        return jnp.zeros_like(value)
    return lax.ppermute(value, axis, pairs)


def take(values, along_axis, start, stop, stride=1):
    return lax.slice_in_dim(values, start, stop, stride, along_axis)


def restrict(values, along_axis, low, out_low, out_high):
    count = out_high - out_low
    first = 2 * out_low - 1 - low
    left = take(values, along_axis, first, first + 2 * count - 1, 2)
    centre = take(values, along_axis, first + 1, first + 2 * count, 2)
    right = take(values, along_axis, first + 2, first + 2 * count + 1, 2)
    return 0.5 * left + centre + 0.5 * right


def restrict_whole(values, along_axis):
    assert along_axis == values.ndim - 1
    cells = values.shape[along_axis]
    fine = lax.broadcasted_iota(jnp.int32, (cells, cells // 2), 0)
    coarse = lax.broadcasted_iota(jnp.int32, (cells, cells // 2), 1)
    distance = fine - 2 * coarse
    matrix = jnp.where(distance == 0, 1.0, jnp.where(jnp.abs(distance) == 1, 0.5, 0.0))
    return jnp.einsum("xyz,zw->xyw", values, matrix.astype(jnp.float32), precision=HIGHEST)


def prolong_whole(coarse_values):
    cells = coarse_values.shape[-1]
    coarse = lax.broadcasted_iota(jnp.int32, (cells, 2 * cells), 0)
    fine = lax.broadcasted_iota(jnp.int32, (cells, 2 * cells), 1)
    matrix = jnp.where(fine == 2 * coarse, 1.0, jnp.where((fine == 2 * coarse + 1) | (fine == 2 * coarse - 1), 0.5, 0.0))
    return jnp.einsum("xyz,zw->xyw", coarse_values, matrix.astype(jnp.float32), precision=HIGHEST)


def inside_mask(values, along_axis, axis_name, tile, low):
    count = lax.axis_size(axis_name)
    shape = [1] * values.ndim
    shape[along_axis] = values.shape[along_axis]
    local = lax.broadcasted_iota(jnp.int32, tuple(shape), along_axis) + low
    global_index = lax.axis_index(axis_name) * tile + local
    return jnp.where(global_index < count * tile, values, jnp.zeros_like(values))


def prolong(coarse, along_axis, fine_count):
    m = fine_count // 2
    have = coarse.shape[along_axis]
    if have < m + 1:
        coarse = jnp.concatenate(
            [coarse, jnp.zeros_like(take(coarse, along_axis, 0, m + 1 - have))], axis=along_axis
        )
    base = take(coarse, along_axis, 0, m)
    following = take(coarse, along_axis, 1, m + 1)
    middle = 0.5 * (base + following)
    paired = jnp.stack([base, middle], axis=along_axis + 1)
    shape = list(base.shape)
    shape[along_axis] = 2 * m
    fine = paired.reshape(shape)
    if fine_count > 2 * m:
        fine = jnp.concatenate([fine, take(coarse, along_axis, m, m + 1)], axis=along_axis)
    return fine


def banded_weights(kernel, depth):
    span = kernel.shape[2]
    radius = span // 2
    offset = (
        lax.broadcasted_iota(jnp.int32, (span, depth, depth), 1)
        - lax.broadcasted_iota(jnp.int32, (span, depth, depth), 2)
        + radius
    )
    one_hot = (offset == lax.broadcasted_iota(jnp.int32, (span, depth, depth), 0)).astype(jnp.float32)
    return jnp.einsum("abc,cij->abij", kernel, one_hot, precision=HIGHEST)


def cutoff_sum(window, kernel):
    span = kernel.shape[0]
    rows_first = window.shape[0] - span + 1
    rows_second = window.shape[1] - span + 1
    weights = banded_weights(kernel, window.shape[2])
    stacked = jnp.stack([take(window, 1, b, b + rows_second) for b in range(span)], axis=2)
    accumulated = None
    for a in range(span):
        term = jnp.einsum(
            "xybz,bzw->xyw", take(stacked, 0, a, a + rows_first), weights[a], precision=HIGHEST
        )
        accumulated = term if accumulated is None else accumulated + term
    return accumulated


def widen_many(arrays, along_axis, axis_name, needs):
    tiles = [a.shape[along_axis] for a in arrays]
    reach = 0
    for tile, (low, high) in zip(tiles, needs):
        reach = max(reach, -(-low // tile), -(-high // tile))
    lower = [[] for _ in arrays]
    upper = [[] for _ in arrays]
    for distance in range(1, reach + 1):
        for direction in (1, -1):
            pieces = []
            for index, (a, tile, (low, high)) in enumerate(zip(arrays, tiles, needs)):
                if direction == 1:
                    start = max(0, distance * tile - low)
                    stop = tile if (distance - 1) * tile < low else start
                else:
                    start = 0
                    stop = min(tile, tile + high - distance * tile) if (distance - 1) * tile < high else 0
                if stop > start:
                    pieces.append((index, take(a, along_axis, start, stop)))
            if not pieces:
                continue
            ndim = pieces[0][1].ndim
            widest = [max(p.shape[d] for _, p in pieces) for d in range(ndim)]
            padded = []
            for _, p in pieces:
                pad = [(0, 0 if d == along_axis else widest[d] - p.shape[d]) for d in range(ndim)]
                padded.append(jnp.pad(p, pad))
            moved = from_behind(jnp.concatenate(padded, axis=along_axis), axis_name, direction * distance)
            offset = 0
            for index, p in pieces:
                size = p.shape[along_axis]
                part = take(moved, along_axis, offset, offset + size)
                part = part[tuple(slice(0, p.shape[d]) for d in range(ndim))]
                offset += size
                if direction == 1:
                    lower[index].insert(0, part)
                else:
                    upper[index].append(part)
    return [
        jnp.concatenate(lower[i] + [a] + upper[i], axis=along_axis) for i, a in enumerate(arrays)
    ]


def gather_all(value, along_axis, axis_name):
    count = lax.axis_size(axis_name)
    if count & (count - 1):
        return lax.all_gather(value, axis_name, axis=along_axis, tiled=True)
    position = lax.axis_index(axis_name)
    step = 1
    while step < count:
        other = lax.ppermute(value, axis_name, [(i, i ^ step) for i in range(count)])
        low_half = (position // step) % 2 == 0
        value = jnp.where(
            low_half,
            jnp.concatenate([value, other], axis=along_axis),
            jnp.concatenate([other, value], axis=along_axis),
        )
        step *= 2
    return value


def top_cells(whole_top, top_kernel, tile_first, tile_second):
    n_first, n_second, depth = whole_top.shape
    padded = jnp.pad(top_kernel, ((tile_first, 0), (tile_second, 0), (0, 0)))
    start_first = n_first - 1 - lax.axis_index("gx") * tile_first
    start_second = n_second - 1 - lax.axis_index("gy") * tile_second
    window = lax.dynamic_slice(
        padded,
        (start_first, start_second, jnp.int32(0)),
        (n_first + tile_first, n_second + tile_second, 2 * depth - 1),
    )
    rows = []
    for j in range(tile_first + 1):
        cols = []
        for i in range(tile_second + 1):
            deep = []
            for z in range(depth):
                deep.append(
                    window[
                        tile_first - j : tile_first - j + n_first,
                        tile_second - i : tile_second - i + n_second,
                        depth - 1 - z : 2 * depth - 1 - z,
                    ]
                )
            cols.append(jnp.stack(deep))
        rows.append(jnp.stack(cols))
    weights = jnp.stack(rows)
    return jnp.einsum("jizabc,abc->jiz", weights, whole_top, precision=HIGHEST)


def body(charges, kernels, top_kernel):
    levels = kernels.shape[0]
    radius = kernels.shape[1] // 2
    tile0_first, tile0_second, depth0 = charges.shape
    tiles_first = [tile0_first >> l for l in range(levels + 1)]
    tiles_second = [tile0_second >> l for l in range(levels + 1)]

    low1 = min(-radius, -(2 ** (levels - 1) - 1))
    high1 = tiles_first[1] + radius + 1
    high1_second = tiles_second[1] + radius + 1
    low0 = 2 * low1 - 1
    high0 = 2 * (high1 - 1) + 2
    high0_second = 2 * (high1_second - 1) + 2
    assert -low0 <= tile0_first and high0 - tile0_first <= tile0_first
    assert -low0 <= tile0_second and high0_second - tile0_second <= tile0_second

    below = from_behind(take(charges, 0, tile0_first + low0, tile0_first), "gx", 1)
    above = from_behind(take(charges, 0, 0, high0 - tile0_first), "gx", -1)
    wide = jnp.concatenate([below, charges, above], axis=0)
    below = from_behind(take(wide, 1, tile0_second + low0, tile0_second), "gy", 1)
    above = from_behind(take(wide, 1, 0, high0_second - tile0_second), "gy", -1)
    wide = jnp.concatenate([below, wide, above], axis=1)

    q1 = restrict(wide, 0, low0, low1, high1)
    q1 = restrict(q1, 1, low0, low1, high1_second)
    q1 = restrict_whole(q1, 2)
    q1 = inside_mask(q1, 0, "gx", tiles_first[1], low1)
    q1 = inside_mask(q1, 1, "gy", tiles_second[1], low1)

    coarse = [None, q1]
    low = low1
    current = q1
    for l in range(2, levels + 1):
        new_low = -(2 ** (levels - l) - 1)
        current = restrict(current, 0, low, new_low, tiles_first[l])
        current = restrict(current, 1, low, new_low, tiles_second[l])
        current = restrict_whole(current, 2)
        coarse.append(current)
        low = new_low
    q_top = coarse[levels]

    whole_top = gather_all(gather_all(q_top, 1, "gy"), 0, "gx")

    own = [take(take(coarse[l], 0, 2 ** (levels - l) - 1, 2 ** (levels - l) - 1 + tiles_first[l]), 1,
                2 ** (levels - l) - 1, 2 ** (levels - l) - 1 + tiles_second[l]) for l in range(2, levels)]
    widened = widen_many(own, 0, "gx", [(radius, radius + 1)] * len(own))
    widened = widen_many(widened, 1, "gy", [(radius, radius + 1)] * len(own))

    window0 = take(take(wide, 0, -radius - low0, tile0_first + radius - low0), 1, -radius - low0,
                   tile0_second + radius - low0)
    terms = [cutoff_sum(window0, kernels[0])]
    window1 = take(take(q1, 0, -radius - low1, tiles_first[1] + radius + 1 - low1), 1,
                   -radius - low1, tiles_second[1] + radius + 1 - low1)
    terms.append(cutoff_sum(window1, kernels[1]))
    for l in range(2, levels):
        terms.append(cutoff_sum(widened[l - 2], kernels[l]))

    potential = top_cells(whole_top, top_kernel, tiles_first[levels], tiles_second[levels])
    potential = inside_mask(potential, 0, "gx", tiles_first[levels], 0)
    potential = inside_mask(potential, 1, "gy", tiles_second[levels], 0)
    for l in reversed(range(levels)):
        rim = 1 if l > 0 else 0
        expanded = prolong(potential, 0, tiles_first[l] + rim)
        expanded = prolong(expanded, 1, tiles_second[l] + rim)
        expanded = prolong_whole(expanded)
        potential = terms[l] + expanded
        if rim:
            potential = inside_mask(potential, 0, "gx", tiles_first[l], 0)
            potential = inside_mask(potential, 1, "gy", tiles_second[l], 0)
    return potential


def solution(mesh):
    in_specs = (P("gx", "gy", None), P(), P())
    out_specs = P("gx", "gy", None)
    return jax.shard_map(body, mesh=mesh, in_specs=in_specs, out_specs=out_specs, check_vma=False)
```

```python
import jax
import jax.numpy as jnp
import numpy as np
from jax import lax
from jax.sharding import PartitionSpec as P

HIGHEST = lax.Precision.HIGHEST


def from_behind(value, axis, steps):
    count = lax.axis_size(axis)
    leading, last = (max(0, -steps), min(count, count - steps))
    pairs = [(source, source + steps) for source in range(leading, last)]
    if not pairs:
        return jnp.zeros_like(value)
    return lax.ppermute(value, axis, pairs)


def take(values, along_axis, start, stop, stride=1):
    return lax.slice_in_dim(values, start, stop, stride, along_axis)


def restrict(values, along_axis, low, out_low, out_high):
    count = out_high - out_low
    first = 2 * out_low - 1 - low
    left = take(values, along_axis, first, first + 2 * count - 1, 2)
    centre = take(values, along_axis, first + 1, first + 2 * count, 2)
    right = take(values, along_axis, first + 2, first + 2 * count + 1, 2)
    return 0.5 * left + centre + 0.5 * right


def restrict_whole(values, along_axis):
    assert along_axis == values.ndim - 1
    cells = values.shape[along_axis]
    fine = lax.broadcasted_iota(jnp.int32, (cells, cells // 2), 0)
    coarse = lax.broadcasted_iota(jnp.int32, (cells, cells // 2), 1)
    distance = fine - 2 * coarse
    matrix = jnp.where(distance == 0, 1.0, jnp.where(jnp.abs(distance) == 1, 0.5, 0.0))
    return jnp.einsum("xyz,zw->xyw", values, matrix.astype(jnp.float32), precision=HIGHEST)


def prolong_whole(coarse_values):
    cells = coarse_values.shape[-1]
    coarse = lax.broadcasted_iota(jnp.int32, (cells, 2 * cells), 0)
    fine = lax.broadcasted_iota(jnp.int32, (cells, 2 * cells), 1)
    matrix = jnp.where(fine == 2 * coarse, 1.0, jnp.where((fine == 2 * coarse + 1) | (fine == 2 * coarse - 1), 0.5, 0.0))
    return jnp.einsum("xyz,zw->xyw", coarse_values, matrix.astype(jnp.float32), precision=HIGHEST)


def inside_mask(values, along_axis, axis_name, tile, low):
    count = lax.axis_size(axis_name)
    shape = [1] * values.ndim
    shape[along_axis] = values.shape[along_axis]
    local = lax.broadcasted_iota(jnp.int32, tuple(shape), along_axis) + low
    global_index = lax.axis_index(axis_name) * tile + local
    return jnp.where(global_index < count * tile, values, jnp.zeros_like(values))


def prolong(coarse, along_axis, fine_count):
    m = fine_count // 2
    have = coarse.shape[along_axis]
    if have < m + 1:
        coarse = jnp.concatenate(
            [coarse, jnp.zeros_like(take(coarse, along_axis, 0, m + 1 - have))], axis=along_axis
        )
    base = take(coarse, along_axis, 0, m)
    following = take(coarse, along_axis, 1, m + 1)
    middle = 0.5 * (base + following)
    paired = jnp.stack([base, middle], axis=along_axis + 1)
    shape = list(base.shape)
    shape[along_axis] = 2 * m
    fine = paired.reshape(shape)
    if fine_count > 2 * m:
        fine = jnp.concatenate([fine, take(coarse, along_axis, m, m + 1)], axis=along_axis)
    return fine


def banded_weights(kernel, depth):
    span = kernel.shape[2]
    radius = span // 2
    offset = np.arange(depth)[:, None] - np.arange(depth)[None, :] + radius
    band = (offset[None] == np.arange(span)[:, None, None]).astype(np.float32)
    band = jnp.asarray(np.concatenate([band] * 3, axis=0), dtype=jnp.bfloat16)
    high = lax.reduce_precision(kernel, exponent_bits=8, mantissa_bits=7)
    rest = kernel - high
    middle = lax.reduce_precision(rest, exponent_bits=8, mantissa_bits=7)
    low = rest - middle
    parts = jnp.concatenate([high, middle, low], axis=2).astype(jnp.bfloat16)
    return jnp.einsum("abc,cij->abij", parts, band, preferred_element_type=jnp.float32)


def cutoff_sum(window, kernel):
    span = kernel.shape[0]
    rows_first = window.shape[0] - span + 1
    rows_second = window.shape[1] - span + 1
    weights = banded_weights(kernel, window.shape[2])
    stacked = jnp.stack([take(window, 1, b, b + rows_second) for b in range(span)], axis=2)
    accumulated = None
    for a in range(span):
        term = jnp.einsum(
            "xybz,bzw->xyw", take(stacked, 0, a, a + rows_first), weights[a], precision=HIGHEST
        )
        accumulated = term if accumulated is None else accumulated + term
    return accumulated


def widen_many(arrays, along_axis, axis_name, needs):
    tiles = [a.shape[along_axis] for a in arrays]
    reach = 0
    for tile, (low, high) in zip(tiles, needs):
        reach = max(reach, -(-low // tile), -(-high // tile))
    lower = [[] for _ in arrays]
    upper = [[] for _ in arrays]
    for distance in range(1, reach + 1):
        for direction in (1, -1):
            pieces = []
            for index, (a, tile, (low, high)) in enumerate(zip(arrays, tiles, needs)):
                if direction == 1:
                    start = max(0, distance * tile - low)
                    stop = tile if (distance - 1) * tile < low else start
                else:
                    start = 0
                    stop = min(tile, tile + high - distance * tile) if (distance - 1) * tile < high else 0
                if stop > start:
                    pieces.append((index, take(a, along_axis, start, stop)))
            if not pieces:
                continue
            ndim = pieces[0][1].ndim
            widest = [max(p.shape[d] for _, p in pieces) for d in range(ndim)]
            padded = []
            for _, p in pieces:
                pad = [(0, 0 if d == along_axis else widest[d] - p.shape[d]) for d in range(ndim)]
                padded.append(jnp.pad(p, pad))
            moved = from_behind(jnp.concatenate(padded, axis=along_axis), axis_name, direction * distance)
            offset = 0
            for index, p in pieces:
                size = p.shape[along_axis]
                part = take(moved, along_axis, offset, offset + size)
                part = part[tuple(slice(0, p.shape[d]) for d in range(ndim))]
                offset += size
                if direction == 1:
                    lower[index].insert(0, part)
                else:
                    upper[index].append(part)
    return [
        jnp.concatenate(lower[i] + [a] + upper[i], axis=along_axis) for i, a in enumerate(arrays)
    ]


def gather_all(value, along_axis, axis_name):
    count = lax.axis_size(axis_name)
    if count & (count - 1):
        return lax.all_gather(value, axis_name, axis=along_axis, tiled=True)
    position = lax.axis_index(axis_name)
    step = 1
    while step < count:
        other = lax.ppermute(value, axis_name, [(i, i ^ step) for i in range(count)])
        low_half = (position // step) % 2 == 0
        value = jnp.where(
            low_half,
            jnp.concatenate([value, other], axis=along_axis),
            jnp.concatenate([other, value], axis=along_axis),
        )
        step *= 2
    return value


def top_cells(whole_top, top_kernel, tile_first, tile_second):
    n_first, n_second, depth = whole_top.shape
    padded = jnp.pad(top_kernel, ((tile_first, 0), (tile_second, 0), (0, 0)))
    start_first = n_first - 1 - lax.axis_index("gx") * tile_first
    start_second = n_second - 1 - lax.axis_index("gy") * tile_second
    window = lax.dynamic_slice(
        padded,
        (start_first, start_second, jnp.int32(0)),
        (n_first + tile_first, n_second + tile_second, 2 * depth - 1),
    )
    rows = []
    for j in range(tile_first + 1):
        cols = []
        for i in range(tile_second + 1):
            deep = []
            for z in range(depth):
                deep.append(
                    window[
                        tile_first - j : tile_first - j + n_first,
                        tile_second - i : tile_second - i + n_second,
                        depth - 1 - z : 2 * depth - 1 - z,
                    ]
                )
            cols.append(jnp.stack(deep))
        rows.append(jnp.stack(cols))
    weights = jnp.stack(rows)
    return jnp.einsum("jizabc,abc->jiz", weights, whole_top, precision=HIGHEST)


def body(charges, kernels, top_kernel):
    levels = kernels.shape[0]
    radius = kernels.shape[1] // 2
    tile0_first, tile0_second, depth0 = charges.shape
    tiles_first = [tile0_first >> l for l in range(levels + 1)]
    tiles_second = [tile0_second >> l for l in range(levels + 1)]

    low1 = min(-radius, -(2 ** (levels - 1) - 1))
    high1 = tiles_first[1] + radius + 1
    high1_second = tiles_second[1] + radius + 1
    low0 = 2 * low1 - 1
    high0 = 2 * (high1 - 1) + 2
    high0_second = 2 * (high1_second - 1) + 2
    assert -low0 <= tile0_first and high0 - tile0_first <= tile0_first
    assert -low0 <= tile0_second and high0_second - tile0_second <= tile0_second

    below = from_behind(take(charges, 0, tile0_first + low0, tile0_first), "gx", 1)
    above = from_behind(take(charges, 0, 0, high0 - tile0_first), "gx", -1)
    wide = jnp.concatenate([below, charges, above], axis=0)
    below = from_behind(take(wide, 1, tile0_second + low0, tile0_second), "gy", 1)
    above = from_behind(take(wide, 1, 0, high0_second - tile0_second), "gy", -1)
    wide = jnp.concatenate([below, wide, above], axis=1)

    q1 = restrict(wide, 0, low0, low1, high1)
    q1 = restrict(q1, 1, low0, low1, high1_second)
    q1 = restrict_whole(q1, 2)
    q1 = inside_mask(q1, 0, "gx", tiles_first[1], low1)
    q1 = inside_mask(q1, 1, "gy", tiles_second[1], low1)

    coarse = [None, q1]
    low = low1
    current = q1
    for l in range(2, levels + 1):
        new_low = -(2 ** (levels - l) - 1)
        current = restrict(current, 0, low, new_low, tiles_first[l])
        current = restrict(current, 1, low, new_low, tiles_second[l])
        current = restrict_whole(current, 2)
        coarse.append(current)
        low = new_low
    q_top = coarse[levels]

    whole_top = gather_all(gather_all(q_top, 1, "gy"), 0, "gx")

    own = [take(take(coarse[l], 0, 2 ** (levels - l) - 1, 2 ** (levels - l) - 1 + tiles_first[l]), 1,
                2 ** (levels - l) - 1, 2 ** (levels - l) - 1 + tiles_second[l]) for l in range(2, levels)]
    widened = widen_many(own, 0, "gx", [(radius, radius + 1)] * len(own))
    widened = widen_many(widened, 1, "gy", [(radius, radius + 1)] * len(own))

    window0 = take(take(wide, 0, -radius - low0, tile0_first + radius - low0), 1, -radius - low0,
                   tile0_second + radius - low0)
    terms = [cutoff_sum(window0, kernels[0])]
    window1 = take(take(q1, 0, -radius - low1, tiles_first[1] + radius + 1 - low1), 1,
                   -radius - low1, tiles_second[1] + radius + 1 - low1)
    terms.append(cutoff_sum(window1, kernels[1]))
    for l in range(2, levels):
        terms.append(cutoff_sum(widened[l - 2], kernels[l]))

    potential = top_cells(whole_top, top_kernel, tiles_first[levels], tiles_second[levels])
    potential = inside_mask(potential, 0, "gx", tiles_first[levels], 0)
    potential = inside_mask(potential, 1, "gy", tiles_second[levels], 0)
    for l in reversed(range(levels)):
        rim = 1 if l > 0 else 0
        expanded = prolong(potential, 0, tiles_first[l] + rim)
        expanded = prolong(expanded, 1, tiles_second[l] + rim)
        expanded = prolong_whole(expanded)
        potential = terms[l] + expanded
        if rim:
            potential = inside_mask(potential, 0, "gx", tiles_first[l], 0)
            potential = inside_mask(potential, 1, "gy", tiles_second[l], 0)
    return potential


def solution(mesh):
    in_specs = (P("gx", "gy", None), P(), P())
    out_specs = P("gx", "gy", None)
    return jax.shard_map(body, mesh=mesh, in_specs=in_specs, out_specs=out_specs, check_vma=False)
```

```python
import jax
import jax.numpy as jnp
import numpy as np
from jax import lax
from jax.sharding import PartitionSpec as P

HIGHEST = lax.Precision.HIGHEST


def from_behind(value, axis, steps):
    count = lax.axis_size(axis)
    leading, last = (max(0, -steps), min(count, count - steps))
    pairs = [(source, source + steps) for source in range(leading, last)]
    if not pairs:
        return jnp.zeros_like(value)
    return lax.ppermute(value, axis, pairs)


def take(values, along_axis, start, stop, stride=1):
    return lax.slice_in_dim(values, start, stop, stride, along_axis)


def restrict(values, along_axis, low, out_low, out_high):
    count = out_high - out_low
    first = 2 * out_low - 1 - low
    left = take(values, along_axis, first, first + 2 * count - 1, 2)
    centre = take(values, along_axis, first + 1, first + 2 * count, 2)
    right = take(values, along_axis, first + 2, first + 2 * count + 1, 2)
    return 0.5 * left + centre + 0.5 * right


def restrict_whole(values, along_axis):
    assert along_axis == values.ndim - 1
    cells = values.shape[along_axis]
    fine = lax.broadcasted_iota(jnp.int32, (cells, cells // 2), 0)
    coarse = lax.broadcasted_iota(jnp.int32, (cells, cells // 2), 1)
    distance = fine - 2 * coarse
    matrix = jnp.where(distance == 0, 1.0, jnp.where(jnp.abs(distance) == 1, 0.5, 0.0))
    return jnp.einsum("xyz,zw->xyw", values, matrix.astype(jnp.float32), precision=HIGHEST)


def prolong_whole(coarse_values):
    cells = coarse_values.shape[-1]
    coarse = lax.broadcasted_iota(jnp.int32, (cells, 2 * cells), 0)
    fine = lax.broadcasted_iota(jnp.int32, (cells, 2 * cells), 1)
    matrix = jnp.where(fine == 2 * coarse, 1.0, jnp.where((fine == 2 * coarse + 1) | (fine == 2 * coarse - 1), 0.5, 0.0))
    return jnp.einsum("xyz,zw->xyw", coarse_values, matrix.astype(jnp.float32), precision=HIGHEST)


def inside_mask(values, along_axis, axis_name, tile, low):
    count = lax.axis_size(axis_name)
    shape = [1] * values.ndim
    shape[along_axis] = values.shape[along_axis]
    local = lax.broadcasted_iota(jnp.int32, tuple(shape), along_axis) + low
    global_index = lax.axis_index(axis_name) * tile + local
    return jnp.where(global_index < count * tile, values, jnp.zeros_like(values))


def prolong(coarse, along_axis, fine_count):
    m = fine_count // 2
    have = coarse.shape[along_axis]
    if have < m + 1:
        coarse = jnp.concatenate(
            [coarse, jnp.zeros_like(take(coarse, along_axis, 0, m + 1 - have))], axis=along_axis
        )
    base = take(coarse, along_axis, 0, m)
    following = take(coarse, along_axis, 1, m + 1)
    middle = 0.5 * (base + following)
    paired = jnp.stack([base, middle], axis=along_axis + 1)
    shape = list(base.shape)
    shape[along_axis] = 2 * m
    fine = paired.reshape(shape)
    if fine_count > 2 * m:
        fine = jnp.concatenate([fine, take(coarse, along_axis, m, m + 1)], axis=along_axis)
    return fine


def banded_weights(kernel, depth):
    span = kernel.shape[2]
    radius = span // 2
    offset = np.arange(depth)[:, None] - np.arange(depth)[None, :] + radius
    band = (offset[None] == np.arange(span)[:, None, None]).astype(np.float32)
    band = jnp.asarray(np.concatenate([band] * 3, axis=0), dtype=jnp.bfloat16)
    high = lax.reduce_precision(kernel, exponent_bits=8, mantissa_bits=7)
    rest = kernel - high
    middle = lax.reduce_precision(rest, exponent_bits=8, mantissa_bits=7)
    low = rest - middle
    parts = jnp.concatenate([high, middle, low], axis=2).astype(jnp.bfloat16)
    return [
        jnp.einsum("bc,cij->bij", parts[a], band, preferred_element_type=jnp.float32)
        for a in range(kernel.shape[0])
    ]


def cutoff_sum(window, kernel):
    span = kernel.shape[0]
    rows_first = window.shape[0] - span + 1
    rows_second = window.shape[1] - span + 1
    weights = banded_weights(kernel, window.shape[2])
    stacked = jnp.stack([take(window, 1, b, b + rows_second) for b in range(span)], axis=2)
    accumulated = None
    for a in range(span):
        term = jnp.einsum(
            "xybz,bzw->xyw", take(stacked, 0, a, a + rows_first), weights[a], precision=HIGHEST
        )
        accumulated = term if accumulated is None else accumulated + term
    return accumulated


def widen_many(arrays, along_axis, axis_name, needs):
    tiles = [a.shape[along_axis] for a in arrays]
    reach = 0
    for tile, (low, high) in zip(tiles, needs):
        reach = max(reach, -(-low // tile), -(-high // tile))
    lower = [[] for _ in arrays]
    upper = [[] for _ in arrays]
    for distance in range(1, reach + 1):
        for direction in (1, -1):
            pieces = []
            for index, (a, tile, (low, high)) in enumerate(zip(arrays, tiles, needs)):
                if direction == 1:
                    start = max(0, distance * tile - low)
                    stop = tile if (distance - 1) * tile < low else start
                else:
                    start = 0
                    stop = min(tile, tile + high - distance * tile) if (distance - 1) * tile < high else 0
                if stop > start:
                    pieces.append((index, take(a, along_axis, start, stop)))
            if not pieces:
                continue
            ndim = pieces[0][1].ndim
            widest = [max(p.shape[d] for _, p in pieces) for d in range(ndim)]
            padded = []
            for _, p in pieces:
                pad = [(0, 0 if d == along_axis else widest[d] - p.shape[d]) for d in range(ndim)]
                padded.append(jnp.pad(p, pad))
            moved = from_behind(jnp.concatenate(padded, axis=along_axis), axis_name, direction * distance)
            offset = 0
            for index, p in pieces:
                size = p.shape[along_axis]
                part = take(moved, along_axis, offset, offset + size)
                part = part[tuple(slice(0, p.shape[d]) for d in range(ndim))]
                offset += size
                if direction == 1:
                    lower[index].insert(0, part)
                else:
                    upper[index].append(part)
    return [
        jnp.concatenate(lower[i] + [a] + upper[i], axis=along_axis) for i, a in enumerate(arrays)
    ]


def gather_all(value, along_axis, axis_name):
    count = lax.axis_size(axis_name)
    if count & (count - 1):
        return lax.all_gather(value, axis_name, axis=along_axis, tiled=True)
    position = lax.axis_index(axis_name)
    step = 1
    while step < count:
        other = lax.ppermute(value, axis_name, [(i, i ^ step) for i in range(count)])
        low_half = (position // step) % 2 == 0
        value = jnp.where(
            low_half,
            jnp.concatenate([value, other], axis=along_axis),
            jnp.concatenate([other, value], axis=along_axis),
        )
        step *= 2
    return value


def top_cells(whole_top, top_kernel, tile_first, tile_second):
    n_first, n_second, depth = whole_top.shape
    padded = jnp.pad(top_kernel, ((tile_first, 0), (tile_second, 0), (0, 0)))
    start_first = n_first - 1 - lax.axis_index("gx") * tile_first
    start_second = n_second - 1 - lax.axis_index("gy") * tile_second
    window = lax.dynamic_slice(
        padded,
        (start_first, start_second, jnp.int32(0)),
        (n_first + tile_first, n_second + tile_second, 2 * depth - 1),
    )
    rows = []
    for j in range(tile_first + 1):
        cols = []
        for i in range(tile_second + 1):
            deep = []
            for z in range(depth):
                deep.append(
                    window[
                        tile_first - j : tile_first - j + n_first,
                        tile_second - i : tile_second - i + n_second,
                        depth - 1 - z : 2 * depth - 1 - z,
                    ]
                )
            cols.append(jnp.stack(deep))
        rows.append(jnp.stack(cols))
    weights = jnp.stack(rows)
    return jnp.einsum("jizabc,abc->jiz", weights, whole_top, precision=HIGHEST)


def body(charges, kernels, top_kernel):
    levels = kernels.shape[0]
    radius = kernels.shape[1] // 2
    tile0_first, tile0_second, depth0 = charges.shape
    tiles_first = [tile0_first >> l for l in range(levels + 1)]
    tiles_second = [tile0_second >> l for l in range(levels + 1)]

    low1 = min(-radius, -(2 ** (levels - 1) - 1))
    high1 = tiles_first[1] + radius + 1
    high1_second = tiles_second[1] + radius + 1
    low0 = 2 * low1 - 1
    high0 = 2 * (high1 - 1) + 2
    high0_second = 2 * (high1_second - 1) + 2
    assert -low0 <= tile0_first and high0 - tile0_first <= tile0_first
    assert -low0 <= tile0_second and high0_second - tile0_second <= tile0_second

    below = from_behind(take(charges, 0, tile0_first + low0, tile0_first), "gx", 1)
    above = from_behind(take(charges, 0, 0, high0 - tile0_first), "gx", -1)
    wide = jnp.concatenate([below, charges, above], axis=0)
    below = from_behind(take(wide, 1, tile0_second + low0, tile0_second), "gy", 1)
    above = from_behind(take(wide, 1, 0, high0_second - tile0_second), "gy", -1)
    wide = jnp.concatenate([below, wide, above], axis=1)

    q1 = restrict(wide, 0, low0, low1, high1)
    q1 = restrict(q1, 1, low0, low1, high1_second)
    q1 = restrict_whole(q1, 2)
    q1 = inside_mask(q1, 0, "gx", tiles_first[1], low1)
    q1 = inside_mask(q1, 1, "gy", tiles_second[1], low1)

    coarse = [None, q1]
    low = low1
    current = q1
    for l in range(2, levels + 1):
        new_low = -(2 ** (levels - l) - 1)
        current = restrict(current, 0, low, new_low, tiles_first[l])
        current = restrict(current, 1, low, new_low, tiles_second[l])
        current = restrict_whole(current, 2)
        coarse.append(current)
        low = new_low
    q_top = coarse[levels]

    whole_top = gather_all(gather_all(q_top, 1, "gy"), 0, "gx")

    own = [take(take(coarse[l], 0, 2 ** (levels - l) - 1, 2 ** (levels - l) - 1 + tiles_first[l]), 1,
                2 ** (levels - l) - 1, 2 ** (levels - l) - 1 + tiles_second[l]) for l in range(2, levels)]
    widened = widen_many(own, 0, "gx", [(radius, radius + 1)] * len(own))
    widened = widen_many(widened, 1, "gy", [(radius, radius + 1)] * len(own))

    window0 = take(take(wide, 0, -radius - low0, tile0_first + radius - low0), 1, -radius - low0,
                   tile0_second + radius - low0)
    terms = [cutoff_sum(window0, kernels[0])]
    window1 = take(take(q1, 0, -radius - low1, tiles_first[1] + radius + 1 - low1), 1,
                   -radius - low1, tiles_second[1] + radius + 1 - low1)
    terms.append(cutoff_sum(window1, kernels[1]))
    for l in range(2, levels):
        terms.append(cutoff_sum(widened[l - 2], kernels[l]))

    potential = top_cells(whole_top, top_kernel, tiles_first[levels], tiles_second[levels])
    potential = inside_mask(potential, 0, "gx", tiles_first[levels], 0)
    potential = inside_mask(potential, 1, "gy", tiles_second[levels], 0)
    for l in reversed(range(levels)):
        rim = 1 if l > 0 else 0
        expanded = prolong(potential, 0, tiles_first[l] + rim)
        expanded = prolong(expanded, 1, tiles_second[l] + rim)
        expanded = prolong_whole(expanded)
        potential = terms[l] + expanded
        if rim:
            potential = inside_mask(potential, 0, "gx", tiles_first[l], 0)
            potential = inside_mask(potential, 1, "gy", tiles_second[l], 0)
    return potential


def solution(mesh):
    in_specs = (P("gx", "gy", None), P(), P())
    out_specs = P("gx", "gy", None)
    return jax.shard_map(body, mesh=mesh, in_specs=in_specs, out_specs=out_specs, check_vma=False)
```

```python
import jax
import jax.numpy as jnp
import numpy as np
from jax import lax
from jax.sharding import PartitionSpec as P

HIGHEST = lax.Precision.HIGHEST


def from_behind(value, axis, steps):
    count = lax.axis_size(axis)
    leading, last = (max(0, -steps), min(count, count - steps))
    pairs = [(source, source + steps) for source in range(leading, last)]
    if not pairs:
        return jnp.zeros_like(value)
    return lax.ppermute(value, axis, pairs)


def take(values, along_axis, start, stop, stride=1):
    return lax.slice_in_dim(values, start, stop, stride, along_axis)


def restrict(values, along_axis, low, out_low, out_high):
    count = out_high - out_low
    first = 2 * out_low - 1 - low
    left = take(values, along_axis, first, first + 2 * count - 1, 2)
    centre = take(values, along_axis, first + 1, first + 2 * count, 2)
    right = take(values, along_axis, first + 2, first + 2 * count + 1, 2)
    return 0.5 * left + centre + 0.5 * right


def restrict_whole(values, along_axis):
    assert along_axis == values.ndim - 1
    cells = values.shape[along_axis]
    fine = lax.broadcasted_iota(jnp.int32, (cells, cells // 2), 0)
    coarse = lax.broadcasted_iota(jnp.int32, (cells, cells // 2), 1)
    distance = fine - 2 * coarse
    matrix = jnp.where(distance == 0, 1.0, jnp.where(jnp.abs(distance) == 1, 0.5, 0.0))
    return jnp.einsum("xyz,zw->xyw", values, matrix.astype(jnp.float32), precision=HIGHEST)


def prolong_whole(coarse_values):
    cells = coarse_values.shape[-1]
    coarse = lax.broadcasted_iota(jnp.int32, (cells, 2 * cells), 0)
    fine = lax.broadcasted_iota(jnp.int32, (cells, 2 * cells), 1)
    matrix = jnp.where(fine == 2 * coarse, 1.0, jnp.where((fine == 2 * coarse + 1) | (fine == 2 * coarse - 1), 0.5, 0.0))
    return jnp.einsum("xyz,zw->xyw", coarse_values, matrix.astype(jnp.float32), precision=HIGHEST)


def inside_mask(values, along_axis, axis_name, tile, low):
    count = lax.axis_size(axis_name)
    shape = [1] * values.ndim
    shape[along_axis] = values.shape[along_axis]
    local = lax.broadcasted_iota(jnp.int32, tuple(shape), along_axis) + low
    global_index = lax.axis_index(axis_name) * tile + local
    return jnp.where(global_index < count * tile, values, jnp.zeros_like(values))


def prolong(coarse, along_axis, fine_count):
    m = fine_count // 2
    have = coarse.shape[along_axis]
    if have < m + 1:
        coarse = jnp.concatenate(
            [coarse, jnp.zeros_like(take(coarse, along_axis, 0, m + 1 - have))], axis=along_axis
        )
    base = take(coarse, along_axis, 0, m)
    following = take(coarse, along_axis, 1, m + 1)
    middle = 0.5 * (base + following)
    paired = jnp.stack([base, middle], axis=along_axis + 1)
    shape = list(base.shape)
    shape[along_axis] = 2 * m
    fine = paired.reshape(shape)
    if fine_count > 2 * m:
        fine = jnp.concatenate([fine, take(coarse, along_axis, m, m + 1)], axis=along_axis)
    return fine


def banded_weights(kernel, depth):
    span = kernel.shape[2]
    radius = span // 2
    offset = np.arange(depth)[:, None] - np.arange(depth)[None, :] + radius
    band = (offset[None] == np.arange(span)[:, None, None]).astype(np.float32)
    band = jnp.asarray(np.concatenate([band] * 3, axis=0), dtype=jnp.bfloat16)
    high = lax.reduce_precision(kernel, exponent_bits=8, mantissa_bits=7)
    rest = kernel - high
    middle = lax.reduce_precision(rest, exponent_bits=8, mantissa_bits=7)
    low = rest - middle
    parts = jnp.concatenate([high, middle, low], axis=2).astype(jnp.bfloat16)
    return jnp.einsum("abc,cij->abij", parts, band, preferred_element_type=jnp.float32)


def cutoff_sum(window, kernel):
    span = kernel.shape[0]
    rows_first = window.shape[0] - span + 1
    rows_second = window.shape[1] - span + 1
    weights = banded_weights(kernel, window.shape[2])
    stacked = jnp.stack([take(window, 1, b, b + rows_second) for b in range(span)], axis=2)
    accumulated = None
    for a in range(span):
        term = jnp.einsum(
            "xybz,bzw->xyw", take(stacked, 0, a, a + rows_first), weights[a], precision=lax.Precision.HIGH
        )
        accumulated = term if accumulated is None else accumulated + term
    return accumulated


def widen_many(arrays, along_axis, axis_name, needs):
    tiles = [a.shape[along_axis] for a in arrays]
    reach = 0
    for tile, (low, high) in zip(tiles, needs):
        reach = max(reach, -(-low // tile), -(-high // tile))
    lower = [[] for _ in arrays]
    upper = [[] for _ in arrays]
    for distance in range(1, reach + 1):
        for direction in (1, -1):
            pieces = []
            for index, (a, tile, (low, high)) in enumerate(zip(arrays, tiles, needs)):
                if direction == 1:
                    start = max(0, distance * tile - low)
                    stop = tile if (distance - 1) * tile < low else start
                else:
                    start = 0
                    stop = min(tile, tile + high - distance * tile) if (distance - 1) * tile < high else 0
                if stop > start:
                    pieces.append((index, take(a, along_axis, start, stop)))
            if not pieces:
                continue
            ndim = pieces[0][1].ndim
            widest = [max(p.shape[d] for _, p in pieces) for d in range(ndim)]
            padded = []
            for _, p in pieces:
                pad = [(0, 0 if d == along_axis else widest[d] - p.shape[d]) for d in range(ndim)]
                padded.append(jnp.pad(p, pad))
            moved = from_behind(jnp.concatenate(padded, axis=along_axis), axis_name, direction * distance)
            offset = 0
            for index, p in pieces:
                size = p.shape[along_axis]
                part = take(moved, along_axis, offset, offset + size)
                part = part[tuple(slice(0, p.shape[d]) for d in range(ndim))]
                offset += size
                if direction == 1:
                    lower[index].insert(0, part)
                else:
                    upper[index].append(part)
    return [
        jnp.concatenate(lower[i] + [a] + upper[i], axis=along_axis) for i, a in enumerate(arrays)
    ]


def gather_all(value, along_axis, axis_name):
    count = lax.axis_size(axis_name)
    if count & (count - 1):
        return lax.all_gather(value, axis_name, axis=along_axis, tiled=True)
    position = lax.axis_index(axis_name)
    step = 1
    while step < count:
        other = lax.ppermute(value, axis_name, [(i, i ^ step) for i in range(count)])
        low_half = (position // step) % 2 == 0
        value = jnp.where(
            low_half,
            jnp.concatenate([value, other], axis=along_axis),
            jnp.concatenate([other, value], axis=along_axis),
        )
        step *= 2
    return value


def top_cells(whole_top, top_kernel, tile_first, tile_second):
    n_first, n_second, depth = whole_top.shape
    padded = jnp.pad(top_kernel, ((tile_first, 0), (tile_second, 0), (0, 0)))
    start_first = n_first - 1 - lax.axis_index("gx") * tile_first
    start_second = n_second - 1 - lax.axis_index("gy") * tile_second
    window = lax.dynamic_slice(
        padded,
        (start_first, start_second, jnp.int32(0)),
        (n_first + tile_first, n_second + tile_second, 2 * depth - 1),
    )
    rows = []
    for j in range(tile_first + 1):
        cols = []
        for i in range(tile_second + 1):
            deep = []
            for z in range(depth):
                deep.append(
                    window[
                        tile_first - j : tile_first - j + n_first,
                        tile_second - i : tile_second - i + n_second,
                        depth - 1 - z : 2 * depth - 1 - z,
                    ]
                )
            cols.append(jnp.stack(deep))
        rows.append(jnp.stack(cols))
    weights = jnp.stack(rows)
    return jnp.einsum("jizabc,abc->jiz", weights, whole_top, precision=HIGHEST)


def body(charges, kernels, top_kernel):
    levels = kernels.shape[0]
    radius = kernels.shape[1] // 2
    tile0_first, tile0_second, depth0 = charges.shape
    tiles_first = [tile0_first >> l for l in range(levels + 1)]
    tiles_second = [tile0_second >> l for l in range(levels + 1)]

    low1 = min(-radius, -(2 ** (levels - 1) - 1))
    high1 = tiles_first[1] + radius + 1
    high1_second = tiles_second[1] + radius + 1
    low0 = 2 * low1 - 1
    high0 = 2 * (high1 - 1) + 2
    high0_second = 2 * (high1_second - 1) + 2
    assert -low0 <= tile0_first and high0 - tile0_first <= tile0_first
    assert -low0 <= tile0_second and high0_second - tile0_second <= tile0_second

    below = from_behind(take(charges, 0, tile0_first + low0, tile0_first), "gx", 1)
    above = from_behind(take(charges, 0, 0, high0 - tile0_first), "gx", -1)
    wide = jnp.concatenate([below, charges, above], axis=0)
    below = from_behind(take(wide, 1, tile0_second + low0, tile0_second), "gy", 1)
    above = from_behind(take(wide, 1, 0, high0_second - tile0_second), "gy", -1)
    wide = jnp.concatenate([below, wide, above], axis=1)

    q1 = restrict(wide, 0, low0, low1, high1)
    q1 = restrict(q1, 1, low0, low1, high1_second)
    q1 = restrict_whole(q1, 2)
    q1 = inside_mask(q1, 0, "gx", tiles_first[1], low1)
    q1 = inside_mask(q1, 1, "gy", tiles_second[1], low1)

    coarse = [None, q1]
    low = low1
    current = q1
    for l in range(2, levels + 1):
        new_low = -(2 ** (levels - l) - 1)
        current = restrict(current, 0, low, new_low, tiles_first[l])
        current = restrict(current, 1, low, new_low, tiles_second[l])
        current = restrict_whole(current, 2)
        coarse.append(current)
        low = new_low
    q_top = coarse[levels]

    whole_top = gather_all(gather_all(q_top, 1, "gy"), 0, "gx")

    own = [take(take(coarse[l], 0, 2 ** (levels - l) - 1, 2 ** (levels - l) - 1 + tiles_first[l]), 1,
                2 ** (levels - l) - 1, 2 ** (levels - l) - 1 + tiles_second[l]) for l in range(2, levels)]
    widened = widen_many(own, 0, "gx", [(radius, radius + 1)] * len(own))
    widened = widen_many(widened, 1, "gy", [(radius, radius + 1)] * len(own))

    window0 = take(take(wide, 0, -radius - low0, tile0_first + radius - low0), 1, -radius - low0,
                   tile0_second + radius - low0)
    terms = [cutoff_sum(window0, kernels[0])]
    window1 = take(take(q1, 0, -radius - low1, tiles_first[1] + radius + 1 - low1), 1,
                   -radius - low1, tiles_second[1] + radius + 1 - low1)
    terms.append(cutoff_sum(window1, kernels[1]))
    for l in range(2, levels):
        terms.append(cutoff_sum(widened[l - 2], kernels[l]))

    potential = top_cells(whole_top, top_kernel, tiles_first[levels], tiles_second[levels])
    potential = inside_mask(potential, 0, "gx", tiles_first[levels], 0)
    potential = inside_mask(potential, 1, "gy", tiles_second[levels], 0)
    for l in reversed(range(levels)):
        rim = 1 if l > 0 else 0
        expanded = prolong(potential, 0, tiles_first[l] + rim)
        expanded = prolong(expanded, 1, tiles_second[l] + rim)
        expanded = prolong_whole(expanded)
        potential = terms[l] + expanded
        if rim:
            potential = inside_mask(potential, 0, "gx", tiles_first[l], 0)
            potential = inside_mask(potential, 1, "gy", tiles_second[l], 0)
    return potential


def solution(mesh):
    in_specs = (P("gx", "gy", None), P(), P())
    out_specs = P("gx", "gy", None)
    return jax.shard_map(body, mesh=mesh, in_specs=in_specs, out_specs=out_specs, check_vma=False)
```

```python
import jax
import jax.numpy as jnp
import numpy as np
from jax import lax
from jax.sharding import PartitionSpec as P

HIGHEST = lax.Precision.HIGHEST


def from_behind(value, axis, steps):
    count = lax.axis_size(axis)
    leading, last = (max(0, -steps), min(count, count - steps))
    pairs = [(source, source + steps) for source in range(leading, last)]
    if not pairs:
        return jnp.zeros_like(value)
    return lax.ppermute(value, axis, pairs)


def take(values, along_axis, start, stop, stride=1):
    return lax.slice_in_dim(values, start, stop, stride, along_axis)


def restrict(values, along_axis, low, out_low, out_high):
    count = out_high - out_low
    first = 2 * out_low - 1 - low
    left = take(values, along_axis, first, first + 2 * count - 1, 2)
    centre = take(values, along_axis, first + 1, first + 2 * count, 2)
    right = take(values, along_axis, first + 2, first + 2 * count + 1, 2)
    return 0.5 * left + centre + 0.5 * right


def restrict_whole(values, along_axis):
    assert along_axis == values.ndim - 1
    cells = values.shape[along_axis]
    fine = lax.broadcasted_iota(jnp.int32, (cells, cells // 2), 0)
    coarse = lax.broadcasted_iota(jnp.int32, (cells, cells // 2), 1)
    distance = fine - 2 * coarse
    matrix = jnp.where(distance == 0, 1.0, jnp.where(jnp.abs(distance) == 1, 0.5, 0.0))
    return jnp.einsum("xyz,zw->xyw", values, matrix.astype(jnp.float32), precision=HIGHEST)


def prolong_whole(coarse_values):
    cells = coarse_values.shape[-1]
    coarse = lax.broadcasted_iota(jnp.int32, (cells, 2 * cells), 0)
    fine = lax.broadcasted_iota(jnp.int32, (cells, 2 * cells), 1)
    matrix = jnp.where(fine == 2 * coarse, 1.0, jnp.where((fine == 2 * coarse + 1) | (fine == 2 * coarse - 1), 0.5, 0.0))
    return jnp.einsum("xyz,zw->xyw", coarse_values, matrix.astype(jnp.float32), precision=HIGHEST)


def inside_mask(values, along_axis, axis_name, tile, low):
    count = lax.axis_size(axis_name)
    shape = [1] * values.ndim
    shape[along_axis] = values.shape[along_axis]
    local = lax.broadcasted_iota(jnp.int32, tuple(shape), along_axis) + low
    global_index = lax.axis_index(axis_name) * tile + local
    return jnp.where(global_index < count * tile, values, jnp.zeros_like(values))


def prolong(coarse, along_axis, fine_count):
    m = fine_count // 2
    have = coarse.shape[along_axis]
    if have < m + 1:
        coarse = jnp.concatenate(
            [coarse, jnp.zeros_like(take(coarse, along_axis, 0, m + 1 - have))], axis=along_axis
        )
    base = take(coarse, along_axis, 0, m)
    following = take(coarse, along_axis, 1, m + 1)
    middle = 0.5 * (base + following)
    paired = jnp.stack([base, middle], axis=along_axis + 1)
    shape = list(base.shape)
    shape[along_axis] = 2 * m
    fine = paired.reshape(shape)
    if fine_count > 2 * m:
        fine = jnp.concatenate([fine, take(coarse, along_axis, m, m + 1)], axis=along_axis)
    return fine


def banded_weights(kernel, depth):
    span = kernel.shape[2]
    radius = span // 2
    offset = np.arange(depth)[:, None] - np.arange(depth)[None, :] + radius
    band = (offset[None] == np.arange(span)[:, None, None]).astype(np.float32)
    band = jnp.asarray(np.concatenate([band] * 3, axis=0), dtype=jnp.bfloat16)
    high = lax.reduce_precision(kernel, exponent_bits=8, mantissa_bits=7)
    rest = kernel - high
    middle = lax.reduce_precision(rest, exponent_bits=8, mantissa_bits=7)
    low = rest - middle
    parts = jnp.concatenate([high, middle, low], axis=2).astype(jnp.bfloat16)
    return jnp.einsum("abc,cij->abij", parts, band, preferred_element_type=jnp.float32)


def cutoff_sum(window, kernel):
    span = kernel.shape[0]
    rows_first = window.shape[0] - span + 1
    rows_second = window.shape[1] - span + 1
    weights = banded_weights(kernel, window.shape[2])
    stacked = jnp.stack([take(window, 1, b, b + rows_second) for b in range(span)], axis=2)
    accumulated = None
    for a in range(span):
        term = jnp.einsum(
            "xybz,bzw->xyw", take(stacked, 0, a, a + rows_first), weights[a], precision=lax.Precision.HIGH
        )
        accumulated = term if accumulated is None else accumulated + term
    return accumulated


def widen_many(arrays, along_axis, axis_name, needs):
    tiles = [a.shape[along_axis] for a in arrays]
    reach = 0
    for tile, (low, high) in zip(tiles, needs):
        reach = max(reach, -(-low // tile), -(-high // tile))
    lower = [[] for _ in arrays]
    upper = [[] for _ in arrays]
    for distance in range(1, reach + 1):
        for direction in (1, -1):
            pieces = []
            for index, (a, tile, (low, high)) in enumerate(zip(arrays, tiles, needs)):
                if direction == 1:
                    start = max(0, distance * tile - low)
                    stop = tile if (distance - 1) * tile < low else start
                else:
                    start = 0
                    stop = min(tile, tile + high - distance * tile) if (distance - 1) * tile < high else 0
                if stop > start:
                    pieces.append((index, take(a, along_axis, start, stop)))
            if not pieces:
                continue
            ndim = pieces[0][1].ndim
            widest = [max(p.shape[d] for _, p in pieces) for d in range(ndim)]
            padded = []
            for _, p in pieces:
                pad = [(0, 0 if d == along_axis else widest[d] - p.shape[d]) for d in range(ndim)]
                padded.append(jnp.pad(p, pad))
            moved = from_behind(jnp.concatenate(padded, axis=along_axis), axis_name, direction * distance)
            offset = 0
            for index, p in pieces:
                size = p.shape[along_axis]
                part = take(moved, along_axis, offset, offset + size)
                part = part[tuple(slice(0, p.shape[d]) for d in range(ndim))]
                offset += size
                if direction == 1:
                    lower[index].insert(0, part)
                else:
                    upper[index].append(part)
    return [
        jnp.concatenate(lower[i] + [a] + upper[i], axis=along_axis) for i, a in enumerate(arrays)
    ]


def gather_all(value, along_axis, axis_name):
    count = lax.axis_size(axis_name)
    if count & (count - 1):
        return lax.all_gather(value, axis_name, axis=along_axis, tiled=True)
    position = lax.axis_index(axis_name)
    step = 1
    while step < count:
        other = lax.ppermute(value, axis_name, [(i, i ^ step) for i in range(count)])
        low_half = (position // step) % 2 == 0
        value = jnp.where(
            low_half,
            jnp.concatenate([value, other], axis=along_axis),
            jnp.concatenate([other, value], axis=along_axis),
        )
        step *= 2
    return value


def top_cells(whole_top, top_kernel, tile_first, tile_second):
    n_first, n_second, depth = whole_top.shape
    padded = jnp.pad(top_kernel, ((tile_first, 0), (tile_second, 0), (0, 0)))
    start_first = n_first - 1 - lax.axis_index("gx") * tile_first
    start_second = n_second - 1 - lax.axis_index("gy") * tile_second
    window = lax.dynamic_slice(
        padded,
        (start_first, start_second, jnp.int32(0)),
        (n_first + tile_first, n_second + tile_second, 2 * depth - 1),
    )
    rows = []
    for j in range(tile_first + 1):
        cols = []
        for i in range(tile_second + 1):
            deep = []
            for z in range(depth):
                deep.append(
                    window[
                        tile_first - j : tile_first - j + n_first,
                        tile_second - i : tile_second - i + n_second,
                        depth - 1 - z : 2 * depth - 1 - z,
                    ]
                )
            cols.append(jnp.stack(deep))
        rows.append(jnp.stack(cols))
    weights = jnp.stack(rows)
    return jnp.einsum("jizabc,abc->jiz", weights, whole_top, precision=lax.Precision.HIGH)


def body(charges, kernels, top_kernel):
    levels = kernels.shape[0]
    radius = kernels.shape[1] // 2
    tile0_first, tile0_second, depth0 = charges.shape
    tiles_first = [tile0_first >> l for l in range(levels + 1)]
    tiles_second = [tile0_second >> l for l in range(levels + 1)]

    low1 = min(-radius, -(2 ** (levels - 1) - 1))
    high1 = tiles_first[1] + radius + 1
    high1_second = tiles_second[1] + radius + 1
    low0 = 2 * low1 - 1
    high0 = 2 * (high1 - 1) + 2
    high0_second = 2 * (high1_second - 1) + 2
    assert -low0 <= tile0_first and high0 - tile0_first <= tile0_first
    assert -low0 <= tile0_second and high0_second - tile0_second <= tile0_second

    below = from_behind(take(charges, 0, tile0_first + low0, tile0_first), "gx", 1)
    above = from_behind(take(charges, 0, 0, high0 - tile0_first), "gx", -1)
    wide = jnp.concatenate([below, charges, above], axis=0)
    below = from_behind(take(wide, 1, tile0_second + low0, tile0_second), "gy", 1)
    above = from_behind(take(wide, 1, 0, high0_second - tile0_second), "gy", -1)
    wide = jnp.concatenate([below, wide, above], axis=1)

    q1 = restrict(wide, 0, low0, low1, high1)
    q1 = restrict(q1, 1, low0, low1, high1_second)
    q1 = restrict_whole(q1, 2)
    q1 = inside_mask(q1, 0, "gx", tiles_first[1], low1)
    q1 = inside_mask(q1, 1, "gy", tiles_second[1], low1)

    coarse = [None, q1]
    low = low1
    current = q1
    for l in range(2, levels + 1):
        new_low = -(2 ** (levels - l) - 1)
        current = restrict(current, 0, low, new_low, tiles_first[l])
        current = restrict(current, 1, low, new_low, tiles_second[l])
        current = restrict_whole(current, 2)
        coarse.append(current)
        low = new_low
    q_top = coarse[levels]

    whole_top = gather_all(gather_all(q_top, 1, "gy"), 0, "gx")

    own = [take(take(coarse[l], 0, 2 ** (levels - l) - 1, 2 ** (levels - l) - 1 + tiles_first[l]), 1,
                2 ** (levels - l) - 1, 2 ** (levels - l) - 1 + tiles_second[l]) for l in range(2, levels)]
    widened = widen_many(own, 0, "gx", [(radius, radius + 1)] * len(own))
    widened = widen_many(widened, 1, "gy", [(radius, radius + 1)] * len(own))

    window0 = take(take(wide, 0, -radius - low0, tile0_first + radius - low0), 1, -radius - low0,
                   tile0_second + radius - low0)
    terms = [cutoff_sum(window0, kernels[0])]
    window1 = take(take(q1, 0, -radius - low1, tiles_first[1] + radius + 1 - low1), 1,
                   -radius - low1, tiles_second[1] + radius + 1 - low1)
    terms.append(cutoff_sum(window1, kernels[1]))
    for l in range(2, levels):
        terms.append(cutoff_sum(widened[l - 2], kernels[l]))

    potential = top_cells(whole_top, top_kernel, tiles_first[levels], tiles_second[levels])
    potential = inside_mask(potential, 0, "gx", tiles_first[levels], 0)
    potential = inside_mask(potential, 1, "gy", tiles_second[levels], 0)
    for l in reversed(range(levels)):
        rim = 1 if l > 0 else 0
        expanded = prolong(potential, 0, tiles_first[l] + rim)
        expanded = prolong(expanded, 1, tiles_second[l] + rim)
        expanded = prolong_whole(expanded)
        potential = terms[l] + expanded
        if rim:
            potential = inside_mask(potential, 0, "gx", tiles_first[l], 0)
            potential = inside_mask(potential, 1, "gy", tiles_second[l], 0)
    return potential


def solution(mesh):
    in_specs = (P("gx", "gy", None), P(), P())
    out_specs = P("gx", "gy", None)
    return jax.shard_map(body, mesh=mesh, in_specs=in_specs, out_specs=out_specs, check_vma=False)
```

```python
import jax
import jax.numpy as jnp
import numpy as np
from jax import lax
from jax.sharding import PartitionSpec as P

HIGHEST = lax.Precision.HIGHEST


def from_behind(value, axis, steps):
    count = lax.axis_size(axis)
    leading, last = (max(0, -steps), min(count, count - steps))
    pairs = [(source, source + steps) for source in range(leading, last)]
    if not pairs:
        return jnp.zeros_like(value)
    return lax.ppermute(value, axis, pairs)


def take(values, along_axis, start, stop, stride=1):
    return lax.slice_in_dim(values, start, stop, stride, along_axis)


def restrict(values, along_axis, low, out_low, out_high):
    count = out_high - out_low
    first = 2 * out_low - 1 - low
    left = take(values, along_axis, first, first + 2 * count - 1, 2)
    centre = take(values, along_axis, first + 1, first + 2 * count, 2)
    right = take(values, along_axis, first + 2, first + 2 * count + 1, 2)
    return 0.5 * left + centre + 0.5 * right


def restrict_whole(values, along_axis):
    assert along_axis == values.ndim - 1
    cells = values.shape[along_axis]
    fine = lax.broadcasted_iota(jnp.int32, (cells, cells // 2), 0)
    coarse = lax.broadcasted_iota(jnp.int32, (cells, cells // 2), 1)
    distance = fine - 2 * coarse
    matrix = jnp.where(distance == 0, 1.0, jnp.where(jnp.abs(distance) == 1, 0.5, 0.0))
    return jnp.einsum("xyz,zw->xyw", values, matrix.astype(jnp.float32), precision=lax.Precision.HIGH)


def prolong_whole(coarse_values):
    cells = coarse_values.shape[-1]
    coarse = lax.broadcasted_iota(jnp.int32, (cells, 2 * cells), 0)
    fine = lax.broadcasted_iota(jnp.int32, (cells, 2 * cells), 1)
    matrix = jnp.where(fine == 2 * coarse, 1.0, jnp.where((fine == 2 * coarse + 1) | (fine == 2 * coarse - 1), 0.5, 0.0))
    return jnp.einsum("xyz,zw->xyw", coarse_values, matrix.astype(jnp.float32), precision=lax.Precision.HIGH)


def inside_mask(values, along_axis, axis_name, tile, low):
    count = lax.axis_size(axis_name)
    shape = [1] * values.ndim
    shape[along_axis] = values.shape[along_axis]
    local = lax.broadcasted_iota(jnp.int32, tuple(shape), along_axis) + low
    global_index = lax.axis_index(axis_name) * tile + local
    return jnp.where(global_index < count * tile, values, jnp.zeros_like(values))


def prolong(coarse, along_axis, fine_count):
    m = fine_count // 2
    have = coarse.shape[along_axis]
    if have < m + 1:
        coarse = jnp.concatenate(
            [coarse, jnp.zeros_like(take(coarse, along_axis, 0, m + 1 - have))], axis=along_axis
        )
    base = take(coarse, along_axis, 0, m)
    following = take(coarse, along_axis, 1, m + 1)
    middle = 0.5 * (base + following)
    paired = jnp.stack([base, middle], axis=along_axis + 1)
    shape = list(base.shape)
    shape[along_axis] = 2 * m
    fine = paired.reshape(shape)
    if fine_count > 2 * m:
        fine = jnp.concatenate([fine, take(coarse, along_axis, m, m + 1)], axis=along_axis)
    return fine


def banded_weights(kernel, depth):
    span = kernel.shape[2]
    radius = span // 2
    offset = np.arange(depth)[:, None] - np.arange(depth)[None, :] + radius
    band = (offset[None] == np.arange(span)[:, None, None]).astype(np.float32)
    band = jnp.asarray(np.concatenate([band] * 3, axis=0), dtype=jnp.bfloat16)
    high = lax.reduce_precision(kernel, exponent_bits=8, mantissa_bits=7)
    rest = kernel - high
    middle = lax.reduce_precision(rest, exponent_bits=8, mantissa_bits=7)
    low = rest - middle
    parts = jnp.concatenate([high, middle, low], axis=2).astype(jnp.bfloat16)
    return jnp.einsum("abc,cij->abij", parts, band, preferred_element_type=jnp.float32)


def cutoff_sum(window, kernel):
    span = kernel.shape[0]
    rows_first = window.shape[0] - span + 1
    rows_second = window.shape[1] - span + 1
    weights = banded_weights(kernel, window.shape[2])
    stacked = jnp.stack([take(window, 1, b, b + rows_second) for b in range(span)], axis=2)
    accumulated = None
    for a in range(span):
        term = jnp.einsum(
            "xybz,bzw->xyw", take(stacked, 0, a, a + rows_first), weights[a], precision=lax.Precision.HIGH
        )
        accumulated = term if accumulated is None else accumulated + term
    return accumulated


def widen_many(arrays, along_axis, axis_name, needs):
    tiles = [a.shape[along_axis] for a in arrays]
    reach = 0
    for tile, (low, high) in zip(tiles, needs):
        reach = max(reach, -(-low // tile), -(-high // tile))
    lower = [[] for _ in arrays]
    upper = [[] for _ in arrays]
    for distance in range(1, reach + 1):
        for direction in (1, -1):
            pieces = []
            for index, (a, tile, (low, high)) in enumerate(zip(arrays, tiles, needs)):
                if direction == 1:
                    start = max(0, distance * tile - low)
                    stop = tile if (distance - 1) * tile < low else start
                else:
                    start = 0
                    stop = min(tile, tile + high - distance * tile) if (distance - 1) * tile < high else 0
                if stop > start:
                    pieces.append((index, take(a, along_axis, start, stop)))
            if not pieces:
                continue
            ndim = pieces[0][1].ndim
            widest = [max(p.shape[d] for _, p in pieces) for d in range(ndim)]
            padded = []
            for _, p in pieces:
                pad = [(0, 0 if d == along_axis else widest[d] - p.shape[d]) for d in range(ndim)]
                padded.append(jnp.pad(p, pad))
            moved = from_behind(jnp.concatenate(padded, axis=along_axis), axis_name, direction * distance)
            offset = 0
            for index, p in pieces:
                size = p.shape[along_axis]
                part = take(moved, along_axis, offset, offset + size)
                part = part[tuple(slice(0, p.shape[d]) for d in range(ndim))]
                offset += size
                if direction == 1:
                    lower[index].insert(0, part)
                else:
                    upper[index].append(part)
    return [
        jnp.concatenate(lower[i] + [a] + upper[i], axis=along_axis) for i, a in enumerate(arrays)
    ]


def gather_all(value, along_axis, axis_name):
    count = lax.axis_size(axis_name)
    if count & (count - 1):
        return lax.all_gather(value, axis_name, axis=along_axis, tiled=True)
    position = lax.axis_index(axis_name)
    step = 1
    while step < count:
        other = lax.ppermute(value, axis_name, [(i, i ^ step) for i in range(count)])
        low_half = (position // step) % 2 == 0
        value = jnp.where(
            low_half,
            jnp.concatenate([value, other], axis=along_axis),
            jnp.concatenate([other, value], axis=along_axis),
        )
        step *= 2
    return value


def top_cells(whole_top, top_kernel, tile_first, tile_second):
    n_first, n_second, depth = whole_top.shape
    padded = jnp.pad(top_kernel, ((tile_first, 0), (tile_second, 0), (0, 0)))
    start_first = n_first - 1 - lax.axis_index("gx") * tile_first
    start_second = n_second - 1 - lax.axis_index("gy") * tile_second
    window = lax.dynamic_slice(
        padded,
        (start_first, start_second, jnp.int32(0)),
        (n_first + tile_first, n_second + tile_second, 2 * depth - 1),
    )
    rows = []
    for j in range(tile_first + 1):
        cols = []
        for i in range(tile_second + 1):
            deep = []
            for z in range(depth):
                deep.append(
                    window[
                        tile_first - j : tile_first - j + n_first,
                        tile_second - i : tile_second - i + n_second,
                        depth - 1 - z : 2 * depth - 1 - z,
                    ]
                )
            cols.append(jnp.stack(deep))
        rows.append(jnp.stack(cols))
    weights = jnp.stack(rows)
    return jnp.einsum("jizabc,abc->jiz", weights, whole_top, precision=lax.Precision.HIGH)


def body(charges, kernels, top_kernel):
    levels = kernels.shape[0]
    radius = kernels.shape[1] // 2
    tile0_first, tile0_second, depth0 = charges.shape
    tiles_first = [tile0_first >> l for l in range(levels + 1)]
    tiles_second = [tile0_second >> l for l in range(levels + 1)]

    low1 = min(-radius, -(2 ** (levels - 1) - 1))
    high1 = tiles_first[1] + radius + 1
    high1_second = tiles_second[1] + radius + 1
    low0 = 2 * low1 - 1
    high0 = 2 * (high1 - 1) + 2
    high0_second = 2 * (high1_second - 1) + 2
    assert -low0 <= tile0_first and high0 - tile0_first <= tile0_first
    assert -low0 <= tile0_second and high0_second - tile0_second <= tile0_second

    below = from_behind(take(charges, 0, tile0_first + low0, tile0_first), "gx", 1)
    above = from_behind(take(charges, 0, 0, high0 - tile0_first), "gx", -1)
    wide = jnp.concatenate([below, charges, above], axis=0)
    below = from_behind(take(wide, 1, tile0_second + low0, tile0_second), "gy", 1)
    above = from_behind(take(wide, 1, 0, high0_second - tile0_second), "gy", -1)
    wide = jnp.concatenate([below, wide, above], axis=1)

    q1 = restrict(wide, 0, low0, low1, high1)
    q1 = restrict(q1, 1, low0, low1, high1_second)
    q1 = restrict_whole(q1, 2)
    q1 = inside_mask(q1, 0, "gx", tiles_first[1], low1)
    q1 = inside_mask(q1, 1, "gy", tiles_second[1], low1)

    coarse = [None, q1]
    low = low1
    current = q1
    for l in range(2, levels + 1):
        new_low = -(2 ** (levels - l) - 1)
        current = restrict(current, 0, low, new_low, tiles_first[l])
        current = restrict(current, 1, low, new_low, tiles_second[l])
        current = restrict_whole(current, 2)
        coarse.append(current)
        low = new_low
    q_top = coarse[levels]

    whole_top = gather_all(gather_all(q_top, 1, "gy"), 0, "gx")

    own = [take(take(coarse[l], 0, 2 ** (levels - l) - 1, 2 ** (levels - l) - 1 + tiles_first[l]), 1,
                2 ** (levels - l) - 1, 2 ** (levels - l) - 1 + tiles_second[l]) for l in range(2, levels)]
    widened = widen_many(own, 0, "gx", [(radius, radius + 1)] * len(own))
    widened = widen_many(widened, 1, "gy", [(radius, radius + 1)] * len(own))

    window0 = take(take(wide, 0, -radius - low0, tile0_first + radius - low0), 1, -radius - low0,
                   tile0_second + radius - low0)
    terms = [cutoff_sum(window0, kernels[0])]
    window1 = take(take(q1, 0, -radius - low1, tiles_first[1] + radius + 1 - low1), 1,
                   -radius - low1, tiles_second[1] + radius + 1 - low1)
    terms.append(cutoff_sum(window1, kernels[1]))
    for l in range(2, levels):
        terms.append(cutoff_sum(widened[l - 2], kernels[l]))

    potential = top_cells(whole_top, top_kernel, tiles_first[levels], tiles_second[levels])
    potential = inside_mask(potential, 0, "gx", tiles_first[levels], 0)
    potential = inside_mask(potential, 1, "gy", tiles_second[levels], 0)
    for l in reversed(range(levels)):
        rim = 1 if l > 0 else 0
        expanded = prolong(potential, 0, tiles_first[l] + rim)
        expanded = prolong(expanded, 1, tiles_second[l] + rim)
        expanded = prolong_whole(expanded)
        potential = terms[l] + expanded
        if rim:
            potential = inside_mask(potential, 0, "gx", tiles_first[l], 0)
            potential = inside_mask(potential, 1, "gy", tiles_second[l], 0)
    return potential


def solution(mesh):
    in_specs = (P("gx", "gy", None), P(), P())
    out_specs = P("gx", "gy", None)
    return jax.shard_map(body, mesh=mesh, in_specs=in_specs, out_specs=out_specs, check_vma=False)
```
